128 devices in a mesh: region: 64 (over z, y, x), chan: 2 (over core).
Axes of the slice: x: 4, y: 4, z: 4, core: 2. Of those that a mesh axis runs over, the one named last changes fastest.
Arguments:
- features: bfloat16 [384, 196608], P('chan', 'region'), may hold values from -6 to 6
- gain: float32 [384], P('chan'), may hold values from 0.1 to 1.9
- bias: float32 [384], P('chan'), may hold values from -3 to 3
- live: int32 [64], P('region'), may hold values from 1024 to 3072, as said below
- neighbors: int32 [27, 196608], P(None, 'region'), may hold values from -1 to 196607, as said below
- weights: bfloat16 [27, 384, 384], P(None, 'chan'), may hold values from -0.0625 to 0.0625
- grad_out: bfloat16 [384, 196608], P('chan', 'region'), may hold values from -0.059814453 to 0.059814453
Outputs:
- conv_out: bfloat16 [384, 196608], P('chan', 'region')
- kernel_grad: float32 [27, 384, 384], P(None, 'chan')
The draws below stay inside these ranges and needn't reach their ends.
Inputs may be any that keep to these rules, and one draw needn't show every extreme that they name: One region has all 3072 slots counted live. `neighbors`: an entry [k, i] is -1 or the index of a live site at most 256 away from i; every entry of a site that is not live is -1.
All inputs are finite; a program needn't handle non-finite values.
Results may differ from the reference program's by a relative error of at most 0.0049.
Values may be sent and summed in bfloat16 or wider, within the bound.
No kernel may reach another device: no remote copies, remote signals or barrier semaphores. Data moves between devices by JAX's collectives and lax.ppermute only.
A program may use at most 128 MiB of HBM per device.

```python
import jax
import jax.numpy as jnp
from jax import lax

C = 384
OFFSETS = 27
SITES_DEV = 3072
HALO = 256
SITES = 196608
N_REGION = 64


def live_table(key):
    folded = jax.random.fold_in(key, 11)
    first_key, second_key = jax.random.split(folded)
    counts = jax.random.randint(first_key, (N_REGION,), SITES_DEV // 3, SITES_DEV + 1)
    fullest = jax.random.randint(second_key, (), 0, N_REGION)
    return jnp.where(jnp.arange(N_REGION) == fullest, SITES_DEV, counts).astype(jnp.int32)


def draw_live(key, part):
    return live_table(key)


def draw_neighbors(key, part):
    counts = live_table(key)
    total_sites = SITES_DEV * N_REGION
    site_ids = jnp.arange(total_sites, dtype=jnp.int32)

    def is_alive(position):
        owner = position // SITES_DEV
        within = position % SITES_DEV
        return (within < counts[owner] - HALO) | (within >= SITES_DEV - HALO)
    folded = jax.random.fold_in(key, 23)
    shift_key, keep_key = jax.random.split(folded)
    shifts = jax.random.randint(shift_key, (OFFSETS, total_sites), -HALO, HALO + 1)
    center = OFFSETS // 2
    shifts = shifts.at[0].set(-HALO).at[OFFSETS - 1].set(HALO).at[center].set(0)
    keeper = jax.random.randint(keep_key, (OFFSETS, total_sites), 0, 5) < 2
    keeper = keeper.at[center].set(True)
    target = site_ids[None, :] + shifts
    inside = (target >= 0) & (target < total_sites)
    clipped = jnp.clip(target, 0, total_sites - 1)
    valid = keeper & inside & is_alive(clipped) & is_alive(site_ids)[None, :]
    return jnp.where(valid, target, -1).astype(jnp.int32)


def shard_levels(own_key, dims, cuts, low, high):
    level = 1.0
    for dim, blocks in cuts:
        heights = jax.random.uniform(jax.random.fold_in(jax.random.fold_in(own_key, 6), dim), (blocks,), jnp.float32, low / len(cuts), high / len(cuts))
        level = level * jnp.repeat(jnp.exp(heights), dims[dim] // blocks).reshape((-1,) + (1,) * (len(dims) - 1 - dim))
    return level


def bell_draw(own_key, dims, scale, limit, pieces=(), kind=jnp.bfloat16):
    result = scale * jax.random.normal(own_key, dims, jnp.float32)
    if pieces:
        result = result * shard_levels(own_key, dims, pieces, -0.22, 0.18)
    return jnp.clip(result, -limit, limit).astype(kind)


def setup_inputs(seed: int = 0) -> dict:
    key_list = jax.random.split(jax.random.key(seed), 8)
    features = bell_draw(key_list[0], (C, SITES), 1.0, 6.0, ((0, 2), (1, 64)))
    gain = jnp.clip(1.0 + 0.18 * jax.random.normal(key_list[1], (C,), jnp.float32), 0.1, 1.9)
    bias = bell_draw(key_list[2], (C,), 0.5, 3.0, ((0, 2),), jnp.float32)
    live = draw_live(jax.random.fold_in(key_list[7], 71), 0)
    neighbors = draw_neighbors(jax.random.fold_in(key_list[7], 71), 0)
    weights = bell_draw(key_list[5], (OFFSETS, C, C), (OFFSETS * C) ** -0.5, 0.0625, ((1, 2),))
    grad_out = bell_draw(key_list[6], (C, SITES), 0.01, 0.059814453, ((0, 2), (1, 64)))
    return dict(features=features, gain=gain, bias=bias, live=live, neighbors=neighbors, weights=weights, grad_out=grad_out)


def reference(features, gain, bias, live, neighbors, weights, grad_out):
    channels, sites_all = features.shape
    column = jnp.arange(sites_all, dtype=jnp.int32)
    region_of = column // SITES_DEV
    row_of = column % SITES_DEV
    live_limit = live[region_of] - HALO
    live_mask = ((row_of < live_limit) | (row_of >= SITES_DEV - HALO)).astype(jnp.float32)
    values = features.astype(jnp.float32)
    live_total = jnp.sum(live_mask)
    average = lax.optimization_barrier(jnp.sum(values * live_mask[None, :], axis=1)) / live_total
    centered = (values - average[:, None]) * live_mask[None, :]
    variance = lax.optimization_barrier(jnp.sum(centered * centered, axis=1)) / live_total
    factor = gain * lax.rsqrt(variance + 1e-05)
    activation = (jnp.maximum((values - average[:, None]) * factor[:, None] + bias[:, None], 0.0) * live_mask[None, :]).astype(jnp.bfloat16)

    def offset_step(running, operand):
        kernel, targets = operand
        position = jnp.where(targets < 0, sites_all, targets).astype(jnp.int32)
        picked = jnp.take(activation, position, axis=1, mode='fill', fill_value=0)
        running = running + jnp.dot(kernel, picked, preferred_element_type=jnp.float32)
        grad_piece = lax.dot_general(grad_out, picked, (((1,), (1,)), ((), ())), preferred_element_type=jnp.float32)
        return (running, grad_piece)
    start = jnp.zeros((channels, sites_all), jnp.float32)
    conv_sum, kernel_grad = lax.scan(offset_step, start, (weights, neighbors))
    return (conv_sum.astype(jnp.bfloat16), kernel_grad)
```

```python
import jax
import jax.numpy as jnp
import numpy as np
from jax import lax
from jax.sharding import Mesh
from jax.sharding import PartitionSpec as P

SUB = ("z", "y", "x")


def region_sum(x):
    for axis in reversed(SUB):
        x = lax.psum(x, axis)
    return x


def padded(x, width):
    count = lax.axis_size(SUB)
    length = x.shape[0]
    up = [(i, (i + 1) % count) for i in range(count - 1)]
    down = [(j, i) for i, j in up]
    last = lax.slice_in_dim(x, length - width, length, axis=0)
    first = lax.slice_in_dim(x, 0, width, axis=0)
    before = lax.ppermute(last, SUB, up)
    after = lax.ppermute(first, SUB, down)
    return jnp.concatenate([before, x, after], axis=0)


def per_device(features, gain, bias, live, neighbors, weights, grad_out):
    channels, columns = features.shape
    border = columns // 12
    region_idx = lax.axis_index(SUB)
    column = jnp.arange(columns, dtype=jnp.int32)
    live_limit = live[0] - border
    live_mask = ((column < live_limit) | (column >= columns - border)).astype(jnp.float32)
    values = features.astype(jnp.float32)
    masked = values * live_mask[None, :]
    live_rows = jnp.sum(live_mask)
    totals, live_total = region_sum((jnp.sum(masked, axis=1), live_rows))
    average = totals / live_total
    centered = (values - average[:, None]) * live_mask[None, :]
    variance = region_sum(jnp.sum(centered * centered, axis=1)) / live_total
    factor = gain * lax.rsqrt(variance + 1e-05)
    normed = (
        jnp.maximum((values - average[:, None]) * factor[:, None] + bias[:, None], 0.0)
        * live_mask[None, :]
    )
    site_rows = jnp.transpose(normed).astype(jnp.bfloat16)
    own_chans = lax.all_gather(site_rows, "chan", axis=1, tiled=True)
    gathered = padded(own_chans, border)
    anchor = region_idx * columns - border
    extent = columns + 2 * border

    def offset_step(running, operand):
        kernel, targets = operand
        position = jnp.where(targets < 0, extent, targets - anchor)
        picked = jnp.take(gathered, position, axis=0, mode="fill", fill_value=0)
        running = running + lax.dot_general(
            kernel, picked, (((1,), (1,)), ((), ())), preferred_element_type=jnp.float32
        )
        grad_piece = jnp.dot(grad_out, picked, preferred_element_type=jnp.float32)
        return (running, grad_piece)

    start = jnp.zeros((weights.shape[1], columns), jnp.float32)
    conv_sum, grad_parts = lax.scan(offset_step, start, (weights, neighbors))
    kernel_grad = region_sum(grad_parts)
    return (conv_sum.astype(jnp.bfloat16), kernel_grad)


def sub_mesh(mesh):
    devices = np.asarray(mesh.devices)
    count = devices.shape[0]
    first = devices[:, 0]
    try:
        sizes = [len({d.coords[a] for d in first}) for a in (2, 1, 0)]
    except (AttributeError, IndexError, TypeError):
        sizes = [count, 1, 1]
    if int(np.prod(sizes)) != count:
        sizes = [count, 1, 1]
    return Mesh(devices.reshape(*sizes, devices.shape[1]), SUB + ("chan",))


def solution(mesh):
    sites = ("chan", SUB)
    return jax.shard_map(
        per_device,
        mesh=sub_mesh(mesh),
        in_specs=(
            P(*sites),
            P("chan"),
            P("chan"),
            P(SUB),
            P(None, SUB),
            P(None, "chan", None),
            P(*sites),
        ),
        out_specs=(P(*sites), P(None, "chan", None)),
        check_vma=False,
    )
```

```python
import functools

import jax
import jax.numpy as jnp
import numpy as np
from jax import lax
from jax.experimental import pallas as pl
from jax.experimental.pallas import tpu as pltpu
from jax.sharding import Mesh
from jax.sharding import PartitionSpec as P

SUB = ("z", "y", "x")
BLOCK = 256


def region_sum(x):
    for axis in reversed(SUB):
        x = lax.psum(x, axis)
    return x


def padded(x, width):
    count = lax.axis_size(SUB)
    length = x.shape[1]
    up = [(i, (i + 1) % count) for i in range(count - 1)]
    down = [(j, i) for i, j in up]
    last = lax.slice_in_dim(x, length - width, length, axis=1)
    first = lax.slice_in_dim(x, 0, width, axis=1)
    before = lax.ppermute(last, SUB, up)
    after = lax.ppermute(first, SUB, down)
    return jnp.concatenate([before, x, after], axis=1)


def conv_kernel(rel_ref, act_ref, w_ref, g_ref, out_ref, kg_ref, *, halo, offsets):
    b = pl.program_id(0)
    window = BLOCK + 2 * halo

    @pl.when(b == 0)
    def _():
        kg_ref[...] = jnp.zeros_like(kg_ref)

    start = pl.multiple_of(b * BLOCK, BLOCK)
    win = act_ref[:, pl.ds(start, window)]
    g_blk = g_ref[...]
    rows = lax.broadcasted_iota(jnp.int32, (window, BLOCK), 0)

    def step(k, acc):
        idx = rel_ref[pl.ds(k, 1), :]
        onehot = jnp.where(rows == idx, 1.0, 0.0).astype(jnp.bfloat16)
        picked = jnp.dot(win, onehot, preferred_element_type=jnp.float32).astype(jnp.bfloat16)
        acc = acc + jnp.dot(w_ref[k], picked, preferred_element_type=jnp.float32)
        kg_ref[k] += lax.dot_general(
            g_blk, picked, (((1,), (1,)), ((), ())), preferred_element_type=jnp.float32
        )
        return acc

    acc = lax.fori_loop(0, offsets, step, jnp.zeros(out_ref.shape, jnp.float32))
    out_ref[...] = acc.astype(out_ref.dtype)


def conv_call(rel, act, weights, grad_out, halo):
    offsets, o_ch, c_all = weights.shape
    columns = grad_out.shape[1]
    extent = act.shape[1]
    kern = functools.partial(conv_kernel, halo=halo, offsets=offsets)
    return pl.pallas_call(
        kern,
        grid=(columns // BLOCK,),
        in_specs=[
            pl.BlockSpec((offsets, BLOCK), lambda b: (0, b)),
            pl.BlockSpec((c_all, extent), lambda b: (0, 0)),
            pl.BlockSpec((offsets, o_ch, c_all), lambda b: (0, 0, 0)),
            pl.BlockSpec((o_ch, BLOCK), lambda b: (0, b)),
        ],
        out_specs=[
            pl.BlockSpec((o_ch, BLOCK), lambda b: (0, b)),
            pl.BlockSpec((offsets, o_ch, c_all), lambda b: (0, 0, 0)),
        ],
        out_shape=[
            jax.ShapeDtypeStruct((o_ch, columns), jnp.bfloat16),
            jax.ShapeDtypeStruct((offsets, o_ch, c_all), jnp.float32),
        ],
        compiler_params=pltpu.CompilerParams(
            dimension_semantics=("arbitrary",), vmem_limit_bytes=56 * 1024 * 1024
        ),
    )(rel, act, weights, grad_out)


def per_device(features, gain, bias, live, neighbors, weights, grad_out):
    channels, columns = features.shape
    border = columns // 12
    region_idx = lax.axis_index(SUB)
    column = jnp.arange(columns, dtype=jnp.int32)
    live_limit = live[0] - border
    live_mask = ((column < live_limit) | (column >= columns - border)).astype(jnp.float32)
    values = features.astype(jnp.float32)
    masked = values * live_mask[None, :]
    live_rows = jnp.sum(live_mask)
    totals, live_total = region_sum((jnp.sum(masked, axis=1), live_rows))
    average = totals / live_total
    centered = (values - average[:, None]) * live_mask[None, :]
    variance = region_sum(jnp.sum(centered * centered, axis=1)) / live_total
    factor = gain * lax.rsqrt(variance + 1e-05)
    normed = (
        jnp.maximum((values - average[:, None]) * factor[:, None] + bias[:, None], 0.0)
        * live_mask[None, :]
    ).astype(jnp.bfloat16)
    own_chans = lax.all_gather(normed, "chan", axis=0, tiled=True)
    gathered = padded(own_chans, border)
    anchor = region_idx * columns - border
    block_base = (column // BLOCK) * BLOCK
    rel = jnp.where(neighbors < 0, -1, neighbors - anchor - block_base[None, :])
    conv_out, grad_parts = conv_call(rel, gathered, weights, grad_out, border)
    kernel_grad = lax.psum(grad_parts, SUB)
    return (conv_out, kernel_grad)


def sub_mesh(mesh):
    devices = np.asarray(mesh.devices)
    count = devices.shape[0]
    first = devices[:, 0]
    try:
        sizes = [len({d.coords[a] for d in first}) for a in (2, 1, 0)]
    except (AttributeError, IndexError, TypeError):
        sizes = [count, 1, 1]
    if int(np.prod(sizes)) != count:
        sizes = [count, 1, 1]
    return Mesh(devices.reshape(*sizes, devices.shape[1]), SUB + ("chan",))


def solution(mesh):
    sites = ("chan", SUB)
    return jax.shard_map(
        per_device,
        mesh=sub_mesh(mesh),
        in_specs=(
            P(*sites),
            P("chan"),
            P("chan"),
            P(SUB),
            P(None, SUB),
            P(None, "chan", None),
            P(*sites),
        ),
        out_specs=(P(*sites), P(None, "chan", None)),
        check_vma=False,
    )
```

```python
import functools

import jax
import jax.numpy as jnp
import numpy as np
from jax import lax
from jax.experimental import pallas as pl
from jax.experimental.pallas import tpu as pltpu
from jax.sharding import Mesh
from jax.sharding import PartitionSpec as P

SUB = ("z", "y", "x")
BLOCK = 256
CHUNKS = (9, 7, 5, 4, 2)


def region_sum(x):
    for axis in reversed(SUB):
        x = lax.psum(x, axis)
    return x


def padded(x, width):
    count = lax.axis_size(SUB)
    length = x.shape[1]
    up = [(i, (i + 1) % count) for i in range(count - 1)]
    down = [(j, i) for i, j in up]
    last = lax.slice_in_dim(x, length - width, length, axis=1)
    first = lax.slice_in_dim(x, 0, width, axis=1)
    before = lax.ppermute(last, SUB, up)
    after = lax.ppermute(first, SUB, down)
    return jnp.concatenate([before, x, after], axis=1)


def conv_kernel(*refs, halo, k0, count, first):
    if first:
        rel_ref, act_ref, w_ref, g_ref, out_ref, kg_ref = refs
    else:
        rel_ref, act_ref, w_ref, g_ref, acc_ref, out_ref, kg_ref = refs
    b = pl.program_id(0)
    window = BLOCK + 2 * halo

    @pl.when(b == 0)
    def _():
        kg_ref[...] = jnp.zeros_like(kg_ref)

    start = pl.multiple_of(b * BLOCK, BLOCK)
    win = act_ref[:, pl.ds(start, window)]
    g_blk = g_ref[...]
    rows = lax.broadcasted_iota(jnp.int32, (window, BLOCK), 0)

    def step(k, acc):
        idx = rel_ref[pl.ds(k0 + k, 1), :]
        onehot = jnp.where(rows == idx, 1.0, 0.0).astype(jnp.bfloat16)
        picked = jnp.dot(win, onehot, preferred_element_type=jnp.float32).astype(jnp.bfloat16)
        acc = acc + jnp.dot(w_ref[k0 + k], picked, preferred_element_type=jnp.float32)
        kg_ref[k] += lax.dot_general(
            g_blk, picked, (((1,), (1,)), ((), ())), preferred_element_type=jnp.float32
        )
        return acc

    init = jnp.zeros(out_ref.shape, jnp.float32) if first else acc_ref[...]
    acc = lax.fori_loop(0, count, step, init)
    out_ref[...] = acc.astype(out_ref.dtype)


def conv_call(rel, act, weights, grad_out, acc, halo, k0, count, last):
    offsets, o_ch, c_all = weights.shape
    columns = grad_out.shape[1]
    extent = act.shape[1]
    first = acc is None
    kern = functools.partial(conv_kernel, halo=halo, k0=k0, count=count, first=first)
    site_block = pl.BlockSpec((o_ch, BLOCK), lambda b: (0, b))
    in_specs = [
        pl.BlockSpec((offsets, BLOCK), lambda b: (0, b)),
        pl.BlockSpec((c_all, extent), lambda b: (0, 0)),
        pl.BlockSpec((offsets, o_ch, c_all), lambda b: (0, 0, 0)),
        site_block,
    ]
    args = [rel, act, weights, grad_out]
    aliases = {}
    if not first:
        in_specs.append(site_block)
        args.append(acc)
        if not last:
            aliases = {4: 0}
    out_type = jnp.bfloat16 if last else jnp.float32
    return pl.pallas_call(
        kern,
        grid=(columns // BLOCK,),
        in_specs=in_specs,
        out_specs=[site_block, pl.BlockSpec((count, o_ch, c_all), lambda b: (0, 0, 0))],
        out_shape=[
            jax.ShapeDtypeStruct((o_ch, columns), out_type),
            jax.ShapeDtypeStruct((count, o_ch, c_all), jnp.float32),
        ],
        input_output_aliases=aliases,
        compiler_params=pltpu.CompilerParams(
            dimension_semantics=("arbitrary",), vmem_limit_bytes=56 * 1024 * 1024
        ),
    )(*args)


def per_device(features, gain, bias, live, neighbors, weights, grad_out):
    channels, columns = features.shape
    border = columns // 12
    region_idx = lax.axis_index(SUB)
    column = jnp.arange(columns, dtype=jnp.int32)
    live_limit = live[0] - border
    live_mask = ((column < live_limit) | (column >= columns - border)).astype(jnp.float32)
    values = features.astype(jnp.float32)
    masked = values * live_mask[None, :]
    live_rows = jnp.sum(live_mask)
    totals, live_total = region_sum((jnp.sum(masked, axis=1), live_rows))
    average = totals / live_total
    centered = (values - average[:, None]) * live_mask[None, :]
    variance = region_sum(jnp.sum(centered * centered, axis=1)) / live_total
    factor = gain * lax.rsqrt(variance + 1e-05)
    normed = (
        jnp.maximum((values - average[:, None]) * factor[:, None] + bias[:, None], 0.0)
        * live_mask[None, :]
    ).astype(jnp.bfloat16)
    own_chans = lax.all_gather(normed, "chan", axis=0, tiled=True)
    gathered = padded(own_chans, border)
    anchor = region_idx * columns - border
    block_base = (column // BLOCK) * BLOCK
    rel = jnp.where(neighbors < 0, -1, neighbors - anchor - block_base[None, :])
    acc = None
    pieces = []
    k0 = 0
    for count in CHUNKS:
        acc, part = conv_call(
            rel, gathered, weights, grad_out, acc, border, k0, count, k0 + count == len(weights)
        )
        if pieces:
            part, _ = lax.optimization_barrier((part, pieces[-1]))
        pieces.append(lax.psum(part, SUB))
        k0 += count
    return (acc, jnp.concatenate(pieces, axis=0))


def sub_mesh(mesh):
    devices = np.asarray(mesh.devices)
    count = devices.shape[0]
    first = devices[:, 0]
    try:
        sizes = [len({d.coords[a] for d in first}) for a in (2, 1, 0)]
    except (AttributeError, IndexError, TypeError):
        sizes = [count, 1, 1]
    if int(np.prod(sizes)) != count:
        sizes = [count, 1, 1]
    return Mesh(devices.reshape(*sizes, devices.shape[1]), SUB + ("chan",))


def solution(mesh):
    sites = ("chan", SUB)
    return jax.shard_map(
        per_device,
        mesh=sub_mesh(mesh),
        in_specs=(
            P(*sites),
            P("chan"),
            P("chan"),
            P(SUB),
            P(None, SUB),
            P(None, "chan", None),
            P(*sites),
        ),
        out_specs=(P(*sites), P(None, "chan", None)),
        check_vma=False,
    )
```

```python
import functools

import jax
import jax.numpy as jnp
import numpy as np
from jax import lax
from jax.experimental import pallas as pl
from jax.experimental.pallas import tpu as pltpu
from jax.sharding import Mesh
from jax.sharding import PartitionSpec as P

SUB = ("z", "y", "x")
BLOCK = 256


def region_sum(x):
    for axis in reversed(SUB):
        x = lax.psum(x, axis)
    return x


def padded(x, width):
    count = lax.axis_size(SUB)
    length = x.shape[1]
    up = [(i, (i + 1) % count) for i in range(count - 1)]
    down = [(j, i) for i, j in up]
    last = lax.slice_in_dim(x, length - width, length, axis=1)
    first = lax.slice_in_dim(x, 0, width, axis=1)
    before = lax.ppermute(last, SUB, up)
    after = lax.ppermute(first, SUB, down)
    return jnp.concatenate([before, x, after], axis=1)


def conv_kernel(rel_ref, act_ref, w_ref, g_ref, out_ref, kg_ref, *, halo, offsets):
    b = pl.program_id(0)
    window = BLOCK + 2 * halo

    @pl.when(b == 0)
    def _():
        kg_ref[...] = jnp.zeros_like(kg_ref)

    start = pl.multiple_of(b * BLOCK, BLOCK)
    win = act_ref[:, pl.ds(start, window)]
    g_t = jnp.transpose(g_ref[...])
    rows = lax.broadcasted_iota(jnp.int32, (window, BLOCK), 0)

    def step(k, acc):
        idx = rel_ref[pl.ds(k, 1), :]
        onehot = jnp.where(rows == idx, 1.0, 0.0).astype(jnp.bfloat16)
        picked = jnp.dot(win, onehot, preferred_element_type=jnp.float32).astype(jnp.bfloat16)
        acc = acc + jnp.dot(w_ref[k], picked, preferred_element_type=jnp.float32)
        kg_ref[k] += jnp.dot(picked, g_t, preferred_element_type=jnp.float32)
        return acc

    acc = lax.fori_loop(0, offsets, step, jnp.zeros(out_ref.shape, jnp.float32), unroll=True)
    out_ref[...] = acc.astype(out_ref.dtype)


def conv_call(rel, act, weights, grad_out, halo):
    offsets, o_ch, c_all = weights.shape
    columns = grad_out.shape[1]
    extent = act.shape[1]
    kern = functools.partial(conv_kernel, halo=halo, offsets=offsets)
    return pl.pallas_call(
        kern,
        grid=(columns // BLOCK,),
        in_specs=[
            pl.BlockSpec((offsets, BLOCK), lambda b: (0, b)),
            pl.BlockSpec((c_all, extent), lambda b: (0, 0)),
            pl.BlockSpec((offsets, o_ch, c_all), lambda b: (0, 0, 0)),
            pl.BlockSpec((o_ch, BLOCK), lambda b: (0, b)),
        ],
        out_specs=[
            pl.BlockSpec((o_ch, BLOCK), lambda b: (0, b)),
            pl.BlockSpec((offsets, c_all, o_ch), lambda b: (0, 0, 0)),
        ],
        out_shape=[
            jax.ShapeDtypeStruct((o_ch, columns), jnp.bfloat16),
            jax.ShapeDtypeStruct((offsets, c_all, o_ch), jnp.float32),
        ],
        compiler_params=pltpu.CompilerParams(
            dimension_semantics=("arbitrary",), vmem_limit_bytes=56 * 1024 * 1024
        ),
    )(rel, act, weights, grad_out)


def per_device(features, gain, bias, live, neighbors, weights, grad_out):
    channels, columns = features.shape
    border = columns // 12
    region_idx = lax.axis_index(SUB)
    column = jnp.arange(columns, dtype=jnp.int32)
    live_limit = live[0] - border
    live_mask = ((column < live_limit) | (column >= columns - border)).astype(jnp.float32)
    values = features.astype(jnp.float32)
    masked = values * live_mask[None, :]
    live_rows = jnp.sum(live_mask)
    totals, live_total = region_sum((jnp.sum(masked, axis=1), live_rows))
    average = totals / live_total
    centered = (values - average[:, None]) * live_mask[None, :]
    variance = region_sum(jnp.sum(centered * centered, axis=1)) / live_total
    factor = gain * lax.rsqrt(variance + 1e-05)
    normed = (
        jnp.maximum((values - average[:, None]) * factor[:, None] + bias[:, None], 0.0)
        * live_mask[None, :]
    ).astype(jnp.bfloat16)
    own_chans = lax.all_gather(normed, "chan", axis=0, tiled=True)
    gathered = padded(own_chans, border)
    anchor = region_idx * columns - border
    block_base = (column // BLOCK) * BLOCK
    rel = jnp.where(neighbors < 0, -1, neighbors - anchor - block_base[None, :])
    conv_out, grad_parts = conv_call(rel, gathered, weights, grad_out, border)
    kernel_grad = jnp.swapaxes(lax.psum(grad_parts, SUB), 1, 2)
    return (conv_out, kernel_grad)


def sub_mesh(mesh):
    devices = np.asarray(mesh.devices)
    count = devices.shape[0]
    first = devices[:, 0]
    try:
        sizes = [len({d.coords[a] for d in first}) for a in (2, 1, 0)]
    except (AttributeError, IndexError, TypeError):
        sizes = [count, 1, 1]
    if int(np.prod(sizes)) != count:
        sizes = [count, 1, 1]
    return Mesh(devices.reshape(*sizes, devices.shape[1]), SUB + ("chan",))


def solution(mesh):
    sites = ("chan", SUB)
    return jax.shard_map(
        per_device,
        mesh=sub_mesh(mesh),
        in_specs=(
            P(*sites),
            P("chan"),
            P("chan"),
            P(SUB),
            P(None, SUB),
            P(None, "chan", None),
            P(*sites),
        ),
        out_specs=(P(*sites), P(None, "chan", None)),
        check_vma=False,
    )
```

```python
import functools

import jax
import jax.numpy as jnp
import numpy as np
from jax import lax
from jax.experimental import pallas as pl
from jax.experimental.pallas import tpu as pltpu
from jax.sharding import Mesh
from jax.sharding import PartitionSpec as P

SUB = ("z", "y", "x")
BLOCK = 256


def region_sum(x):
    for axis in reversed(SUB):
        x = lax.psum(x, axis)
    return x


def padded(x, width):
    count = lax.axis_size(SUB)
    length = x.shape[1]
    up = [(i, (i + 1) % count) for i in range(count - 1)]
    down = [(j, i) for i, j in up]
    last = lax.slice_in_dim(x, length - width, length, axis=1)
    first = lax.slice_in_dim(x, 0, width, axis=1)
    before = lax.ppermute(last, SUB, up)
    after = lax.ppermute(first, SUB, down)
    return jnp.concatenate([before, x, after], axis=1)


def conv_kernel(rel_ref, act_ref, w_ref, g_ref, out_ref, kg_ref, *, halo, offsets):
    b = pl.program_id(0)
    window = BLOCK + 2 * halo

    @pl.when(b == 0)
    def _():
        kg_ref[...] = jnp.zeros_like(kg_ref)

    start = pl.multiple_of(b * BLOCK, BLOCK)
    win = act_ref[:, pl.ds(start, window)]
    g_t = jnp.transpose(g_ref[...])
    rows = lax.broadcasted_iota(jnp.int32, (window, BLOCK), 0)

    def step(k, acc):
        idx = rel_ref[pl.ds(k, 1), :]
        onehot = jnp.where(rows == idx, 1.0, 0.0).astype(jnp.bfloat16)
        picked = jnp.dot(win, onehot, preferred_element_type=jnp.float32).astype(jnp.bfloat16)
        acc = acc + jnp.dot(w_ref[k], picked, preferred_element_type=jnp.float32)
        kg_ref[k] += jnp.dot(picked, g_t, preferred_element_type=jnp.float32)
        return acc

    acc = lax.fori_loop(0, offsets, step, jnp.zeros(out_ref.shape, jnp.float32), unroll=True)
    out_ref[...] = acc.astype(out_ref.dtype)


def conv_call(rel, act, weights, grad_out, halo):
    offsets, o_ch, c_all = weights.shape
    columns = grad_out.shape[1]
    extent = act.shape[1]
    kern = functools.partial(conv_kernel, halo=halo, offsets=offsets)
    return pl.pallas_call(
        kern,
        grid=(columns // BLOCK,),
        in_specs=[
            pl.BlockSpec((offsets, BLOCK), lambda b: (0, b)),
            pl.BlockSpec((c_all, extent), lambda b: (0, 0)),
            pl.BlockSpec((offsets, o_ch, c_all), lambda b: (0, 0, 0)),
            pl.BlockSpec((o_ch, BLOCK), lambda b: (0, b)),
        ],
        out_specs=[
            pl.BlockSpec((o_ch, BLOCK), lambda b: (0, b)),
            pl.BlockSpec((offsets, c_all, o_ch), lambda b: (0, 0, 0)),
        ],
        out_shape=[
            jax.ShapeDtypeStruct((o_ch, columns), jnp.bfloat16),
            jax.ShapeDtypeStruct((offsets, c_all, o_ch), jnp.float32),
        ],
        compiler_params=pltpu.CompilerParams(
            dimension_semantics=("arbitrary",), vmem_limit_bytes=56 * 1024 * 1024
        ),
    )(rel, act, weights, grad_out)


def per_device(features, gain, bias, live, neighbors, weights, grad_out):
    channels, columns = features.shape
    border = columns // 12
    region_idx = lax.axis_index(SUB)
    column = jnp.arange(columns, dtype=jnp.int32)
    live_limit = live[0] - border
    live_mask = ((column < live_limit) | (column >= columns - border)).astype(jnp.float32)
    values = features.astype(jnp.float32)
    live_rows = jnp.sum(live_mask)
    local_sum = jnp.sum(values * live_mask[None, :], axis=1)
    local_mean = local_sum / live_rows
    local_dev = (values - local_mean[:, None]) * live_mask[None, :]
    local_sq = jnp.sum(local_dev * local_dev, axis=1)
    stats = jnp.stack([local_sum, local_sq, jnp.broadcast_to(live_rows, local_sum.shape)])
    for axis in reversed(SUB):
        stats = lax.all_gather(stats, axis, axis=0, tiled=True)
    stats = stats.reshape(-1, 3, channels)
    sums, squares, counts = stats[:, 0], stats[:, 1], stats[:, 2]
    live_total = jnp.sum(counts[:, 0])
    average = jnp.sum(sums, axis=0) / live_total
    spread = sums / counts - average[None, :]
    variance = (jnp.sum(squares, axis=0) + jnp.sum(counts * spread * spread, axis=0)) / live_total
    factor = gain * lax.rsqrt(variance + 1e-05)
    normed = (
        jnp.maximum((values - average[:, None]) * factor[:, None] + bias[:, None], 0.0)
        * live_mask[None, :]
    ).astype(jnp.bfloat16)
    own_chans = lax.all_gather(normed, "chan", axis=0, tiled=True)
    gathered = padded(own_chans, border)
    anchor = region_idx * columns - border
    block_base = (column // BLOCK) * BLOCK
    rel = jnp.where(neighbors < 0, -1, neighbors - anchor - block_base[None, :])
    conv_out, grad_parts = conv_call(rel, gathered, weights, grad_out, border)
    kernel_grad = jnp.swapaxes(lax.psum(grad_parts, SUB), 1, 2)
    return (conv_out, kernel_grad)


def sub_mesh(mesh):
    devices = np.asarray(mesh.devices)
    count = devices.shape[0]
    first = devices[:, 0]
    try:
        sizes = [len({d.coords[a] for d in first}) for a in (2, 1, 0)]
    except (AttributeError, IndexError, TypeError):
        sizes = [count, 1, 1]
    if int(np.prod(sizes)) != count:
        sizes = [count, 1, 1]
    return Mesh(devices.reshape(*sizes, devices.shape[1]), SUB + ("chan",))


def solution(mesh):
    sites = ("chan", SUB)
    return jax.shard_map(
        per_device,
        mesh=sub_mesh(mesh),
        in_specs=(
            P(*sites),
            P("chan"),
            P("chan"),
            P(SUB),
            P(None, SUB),
            P(None, "chan", None),
            P(*sites),
        ),
        out_specs=(P(*sites), P(None, "chan", None)),
        check_vma=False,
    )
```

```python
import functools

import jax
import jax.numpy as jnp
import numpy as np
from jax import lax
from jax.experimental import pallas as pl
from jax.experimental.pallas import tpu as pltpu
from jax.sharding import Mesh
from jax.sharding import PartitionSpec as P

SUB = ("z", "y", "x")
BLOCK = 256


def region_sum(x):
    for axis in reversed(SUB):
        x = lax.psum(x, axis)
    return x


def padded(x, width):
    count = lax.axis_size(SUB)
    length = x.shape[1]
    up = [(i, (i + 1) % count) for i in range(count - 1)]
    down = [(j, i) for i, j in up]
    last = lax.slice_in_dim(x, length - width, length, axis=1)
    first = lax.slice_in_dim(x, 0, width, axis=1)
    before = lax.ppermute(last, SUB, up)
    after = lax.ppermute(first, SUB, down)
    return jnp.concatenate([before, x, after], axis=1)


def offset_kernel(rel_ref, act_ref, w_ref, g_ref, out_ref, kg_ref, picked_ref, acc_ref, *, halo, blocks):
    k = pl.program_id(0)
    window = BLOCK + 2 * halo
    rows = lax.broadcasted_iota(jnp.int32, (window, BLOCK), 0)
    for b in range(blocks):
        idx = rel_ref[pl.ds(k, 1), pl.ds(b * BLOCK, BLOCK)]
        onehot = jnp.where(rows == idx, 1.0, 0.0).astype(jnp.bfloat16)
        win = act_ref[:, pl.ds(b * BLOCK, window)]
        picked_ref[:, pl.ds(b * BLOCK, BLOCK)] = jnp.dot(
            win, onehot, preferred_element_type=jnp.float32
        ).astype(jnp.bfloat16)
    picked = picked_ref[...]
    kg_ref[0] = lax.dot_general(
        g_ref[...], picked, (((1,), (1,)), ((), ())), preferred_element_type=jnp.float32
    )
    part = jnp.dot(w_ref[0], picked, preferred_element_type=jnp.float32)

    @pl.when(k == 0)
    def _():
        acc_ref[...] = part

    @pl.when(k > 0)
    def _():
        acc_ref[...] += part

    @pl.when(k == pl.num_programs(0) - 1)
    def _():
        out_ref[...] = acc_ref[...].astype(out_ref.dtype)


def conv_call(rel, act, weights, grad_out, halo):
    offsets, o_ch, c_all = weights.shape
    columns = rel.shape[1]
    extent = act.shape[1]
    kern = functools.partial(offset_kernel, halo=halo, blocks=columns // BLOCK)
    return pl.pallas_call(
        kern,
        grid=(offsets,),
        in_specs=[
            pl.BlockSpec((offsets, columns), lambda k: (0, 0)),
            pl.BlockSpec((c_all, extent), lambda k: (0, 0)),
            pl.BlockSpec((1, o_ch, c_all), lambda k: (k, 0, 0)),
            pl.BlockSpec((o_ch, columns), lambda k: (0, 0)),
        ],
        out_specs=[
            pl.BlockSpec((o_ch, columns), lambda k: (0, 0)),
            pl.BlockSpec((1, o_ch, c_all), lambda k: (k, 0, 0)),
        ],
        out_shape=[
            jax.ShapeDtypeStruct((o_ch, columns), jnp.bfloat16),
            jax.ShapeDtypeStruct((offsets, o_ch, c_all), jnp.float32),
        ],
        scratch_shapes=[
            pltpu.VMEM((c_all, columns), jnp.bfloat16),
            pltpu.VMEM((o_ch, columns), jnp.float32),
        ],
        compiler_params=pltpu.CompilerParams(
            dimension_semantics=("arbitrary",), vmem_limit_bytes=56 * 1024 * 1024
        ),
    )(rel, act, weights, grad_out)


def per_device(features, gain, bias, live, neighbors, weights, grad_out):
    channels, columns = features.shape
    border = columns // 12
    region_idx = lax.axis_index(SUB)
    column = jnp.arange(columns, dtype=jnp.int32)
    live_limit = live[0] - border
    live_mask = ((column < live_limit) | (column >= columns - border)).astype(jnp.float32)
    values = features.astype(jnp.float32)
    live_rows = jnp.sum(live_mask)
    local_sum = jnp.sum(values * live_mask[None, :], axis=1)
    local_mean = local_sum / live_rows
    local_dev = (values - local_mean[:, None]) * live_mask[None, :]
    local_sq = jnp.sum(local_dev * local_dev, axis=1)
    stats = jnp.stack([local_sum, local_sq, jnp.broadcast_to(live_rows, local_sum.shape)])
    for axis in reversed(SUB):
        stats = lax.all_gather(stats, axis, axis=0, tiled=True)
    stats = stats.reshape(-1, 3, channels)
    sums, squares, counts = stats[:, 0], stats[:, 1], stats[:, 2]
    live_total = jnp.sum(counts[:, 0])
    average = jnp.sum(sums, axis=0) / live_total
    spread = sums / counts - average[None, :]
    variance = (jnp.sum(squares, axis=0) + jnp.sum(counts * spread * spread, axis=0)) / live_total
    factor = gain * lax.rsqrt(variance + 1e-05)
    normed = (
        jnp.maximum((values - average[:, None]) * factor[:, None] + bias[:, None], 0.0)
        * live_mask[None, :]
    ).astype(jnp.bfloat16)
    own_chans = lax.all_gather(normed, "chan", axis=0, tiled=True)
    gathered = padded(own_chans, border)
    anchor = region_idx * columns - border
    block_base = (column // BLOCK) * BLOCK
    rel = jnp.where(neighbors < 0, -1, neighbors - anchor - block_base[None, :])
    conv_out, grad_parts = conv_call(rel, gathered, weights, grad_out, border)
    kernel_grad = lax.psum(grad_parts, SUB)
    return (conv_out, kernel_grad)


def sub_mesh(mesh):
    devices = np.asarray(mesh.devices)
    count = devices.shape[0]
    first = devices[:, 0]
    try:
        sizes = [len({d.coords[a] for d in first}) for a in (2, 1, 0)]
    except (AttributeError, IndexError, TypeError):
        sizes = [count, 1, 1]
    if int(np.prod(sizes)) != count:
        sizes = [count, 1, 1]
    return Mesh(devices.reshape(*sizes, devices.shape[1]), SUB + ("chan",))


def solution(mesh):
    sites = ("chan", SUB)
    return jax.shard_map(
        per_device,
        mesh=sub_mesh(mesh),
        in_specs=(
            P(*sites),
            P("chan"),
            P("chan"),
            P(SUB),
            P(None, SUB),
            P(None, "chan", None),
            P(*sites),
        ),
        out_specs=(P(*sites), P(None, "chan", None)),
        check_vma=False,
    )
```

```python
import functools

import jax
import jax.numpy as jnp
import numpy as np
from jax import lax
from jax.experimental import pallas as pl
from jax.experimental.pallas import tpu as pltpu
from jax.sharding import Mesh
from jax.sharding import PartitionSpec as P

SUB = ("z", "y", "x")
BLOCK = 256


def region_sum(x):
    for axis in reversed(SUB):
        x = lax.psum(x, axis)
    return x


def padded(x, width):
    count = lax.axis_size(SUB)
    length = x.shape[1]
    up = [(i, (i + 1) % count) for i in range(count - 1)]
    down = [(j, i) for i, j in up]
    last = lax.slice_in_dim(x, length - width, length, axis=1)
    first = lax.slice_in_dim(x, 0, width, axis=1)
    before = lax.ppermute(last, SUB, up)
    after = lax.ppermute(first, SUB, down)
    return jnp.concatenate([before, x, after], axis=1)


def offset_kernel(rel_ref, act_ref, g_ref, picked_ref, kg_ref, *, halo, blocks):
    k = pl.program_id(0)
    window = BLOCK + 2 * halo
    rows = lax.broadcasted_iota(jnp.int32, (window, BLOCK), 0)
    for b in range(blocks):
        idx = rel_ref[pl.ds(k, 1), pl.ds(b * BLOCK, BLOCK)]
        onehot = jnp.where(rows == idx, 1.0, 0.0).astype(jnp.bfloat16)
        win = act_ref[:, pl.ds(b * BLOCK, window)]
        picked_ref[0, :, pl.ds(b * BLOCK, BLOCK)] = jnp.dot(
            win, onehot, preferred_element_type=jnp.float32
        ).astype(jnp.bfloat16)
    kg_ref[0] = lax.dot_general(
        g_ref[...], picked_ref[0], (((1,), (1,)), ((), ())), preferred_element_type=jnp.float32
    )


def gather_call(rel, act, grad_out, halo):
    offsets, columns = rel.shape
    c_all, extent = act.shape
    o_ch = grad_out.shape[0]
    kern = functools.partial(offset_kernel, halo=halo, blocks=columns // BLOCK)
    return pl.pallas_call(
        kern,
        grid=(offsets,),
        in_specs=[
            pl.BlockSpec((offsets, columns), lambda k: (0, 0)),
            pl.BlockSpec((c_all, extent), lambda k: (0, 0)),
            pl.BlockSpec((o_ch, columns), lambda k: (0, 0)),
        ],
        out_specs=[
            pl.BlockSpec((1, c_all, columns), lambda k: (k, 0, 0)),
            pl.BlockSpec((1, o_ch, c_all), lambda k: (k, 0, 0)),
        ],
        out_shape=[
            jax.ShapeDtypeStruct((offsets, c_all, columns), jnp.bfloat16),
            jax.ShapeDtypeStruct((offsets, o_ch, c_all), jnp.float32),
        ],
        compiler_params=pltpu.CompilerParams(
            dimension_semantics=("arbitrary",), vmem_limit_bytes=56 * 1024 * 1024
        ),
    )(rel, act, grad_out)


def per_device(features, gain, bias, live, neighbors, weights, grad_out):
    channels, columns = features.shape
    border = columns // 12
    region_idx = lax.axis_index(SUB)
    column = jnp.arange(columns, dtype=jnp.int32)
    live_limit = live[0] - border
    live_mask = ((column < live_limit) | (column >= columns - border)).astype(jnp.float32)
    values = features.astype(jnp.float32)
    live_rows = jnp.sum(live_mask)
    local_sum = jnp.sum(values * live_mask[None, :], axis=1)
    local_mean = local_sum / live_rows
    local_dev = (values - local_mean[:, None]) * live_mask[None, :]
    local_sq = jnp.sum(local_dev * local_dev, axis=1)
    stats = jnp.stack([local_sum, local_sq, jnp.broadcast_to(live_rows, local_sum.shape)])
    for axis in reversed(SUB):
        stats = lax.all_gather(stats, axis, axis=0, tiled=True)
    stats = stats.reshape(-1, 3, channels)
    sums, squares, counts = stats[:, 0], stats[:, 1], stats[:, 2]
    live_total = jnp.sum(counts[:, 0])
    average = jnp.sum(sums, axis=0) / live_total
    spread = sums / counts - average[None, :]
    variance = (jnp.sum(squares, axis=0) + jnp.sum(counts * spread * spread, axis=0)) / live_total
    factor = gain * lax.rsqrt(variance + 1e-05)
    normed = (
        jnp.maximum((values - average[:, None]) * factor[:, None] + bias[:, None], 0.0)
        * live_mask[None, :]
    ).astype(jnp.bfloat16)
    own_chans = lax.all_gather(normed, "chan", axis=0, tiled=True)
    gathered = padded(own_chans, border)
    anchor = region_idx * columns - border
    block_base = (column // BLOCK) * BLOCK
    rel = jnp.where(neighbors < 0, -1, neighbors - anchor - block_base[None, :])
    picked, grad_parts = gather_call(rel, gathered, grad_out, border)
    kernel_grad = lax.psum(grad_parts, SUB)
    conv_out = lax.dot_general(
        weights, picked, (((0, 2), (0, 1)), ((), ())), preferred_element_type=jnp.float32
    ).astype(jnp.bfloat16)
    return (conv_out, kernel_grad)


def sub_mesh(mesh):
    devices = np.asarray(mesh.devices)
    count = devices.shape[0]
    first = devices[:, 0]
    try:
        sizes = [len({d.coords[a] for d in first}) for a in (2, 1, 0)]
    except (AttributeError, IndexError, TypeError):
        sizes = [count, 1, 1]
    if int(np.prod(sizes)) != count:
        sizes = [count, 1, 1]
    return Mesh(devices.reshape(*sizes, devices.shape[1]), SUB + ("chan",))


def solution(mesh):
    sites = ("chan", SUB)
    return jax.shard_map(
        per_device,
        mesh=sub_mesh(mesh),
        in_specs=(
            P(*sites),
            P("chan"),
            P("chan"),
            P(SUB),
            P(None, SUB),
            P(None, "chan", None),
            P(*sites),
        ),
        out_specs=(P(*sites), P(None, "chan", None)),
        check_vma=False,
    )
```

```python
import functools

import jax
import jax.numpy as jnp
import numpy as np
from jax import lax
from jax.experimental import pallas as pl
from jax.experimental.pallas import tpu as pltpu
from jax.sharding import Mesh
from jax.sharding import PartitionSpec as P

SUB = ("z", "y", "x")
BLOCK = 256


def region_sum(x):
    for axis in reversed(SUB):
        x = lax.psum(x, axis)
    return x


def halo_pad(x, width, live):
    count = lax.axis_size(SUB)
    length = x.shape[1]
    up = [(i, (i + 1) % count) for i in range(count - 1)]
    down = [(j, i) for i, j in up]
    before = lax.ppermute(x[:, length - width:], SUB, up)
    after = lax.ppermute(x[:, :width], SUB, down)
    next_live = lax.ppermute(live, SUB, down)
    return jnp.concatenate([before, x, after], axis=1), next_live


def offset_kernel(rel_ref, act_ref, g_ref, picked_ref, kg_ref, *, halo, blocks):
    k = pl.program_id(0)
    window = BLOCK + 2 * halo
    rows = lax.broadcasted_iota(jnp.int32, (window, BLOCK), 0)
    for b in range(blocks):
        idx = rel_ref[pl.ds(k, 1), pl.ds(b * BLOCK, BLOCK)]
        onehot = jnp.where(rows == idx, 1.0, 0.0).astype(jnp.bfloat16)
        win = act_ref[:, pl.ds(b * BLOCK, window)]
        picked_ref[0, :, pl.ds(b * BLOCK, BLOCK)] = jnp.dot(
            win, onehot, preferred_element_type=jnp.float32
        ).astype(jnp.bfloat16)
    kg_ref[0] = lax.dot_general(
        g_ref[...], picked_ref[0], (((1,), (1,)), ((), ())), preferred_element_type=jnp.float32
    )


def gather_call(rel, act, grad_out, halo):
    offsets, columns = rel.shape
    c_all, extent = act.shape
    o_ch = grad_out.shape[0]
    kern = functools.partial(offset_kernel, halo=halo, blocks=columns // BLOCK)
    return pl.pallas_call(
        kern,
        grid=(offsets,),
        in_specs=[
            pl.BlockSpec((offsets, columns), lambda k: (0, 0)),
            pl.BlockSpec((c_all, extent), lambda k: (0, 0)),
            pl.BlockSpec((o_ch, columns), lambda k: (0, 0)),
        ],
        out_specs=[
            pl.BlockSpec((1, c_all, columns), lambda k: (k, 0, 0)),
            pl.BlockSpec((1, o_ch, c_all), lambda k: (k, 0, 0)),
        ],
        out_shape=[
            jax.ShapeDtypeStruct((offsets, c_all, columns), jnp.bfloat16),
            jax.ShapeDtypeStruct((offsets, o_ch, c_all), jnp.float32),
        ],
        compiler_params=pltpu.CompilerParams(
            dimension_semantics=("arbitrary",), vmem_limit_bytes=56 * 1024 * 1024
        ),
    )(rel, act, grad_out)


def per_device(features, gain, bias, live, neighbors, weights, grad_out):
    channels, columns = features.shape
    border = columns // 12
    region_idx = lax.axis_index(SUB)
    column = jnp.arange(columns, dtype=jnp.int32)
    raw_pad, next_live = halo_pad(features, border, live)
    table = lax.all_gather(raw_pad, "chan", axis=0, tiled=True).astype(jnp.float32)
    live_limit = live[0] - border
    live_mask = ((column < live_limit) | (column >= columns - border)).astype(jnp.float32)
    values = features.astype(jnp.float32)
    live_rows = jnp.sum(live_mask)
    local_sum = jnp.sum(values * live_mask[None, :], axis=1)
    local_mean = local_sum / live_rows
    local_dev = (values - local_mean[:, None]) * live_mask[None, :]
    local_sq = jnp.sum(local_dev * local_dev, axis=1)
    stats = jnp.stack(
        [local_sum, local_sq, jnp.broadcast_to(live_rows, local_sum.shape), gain, bias]
    )
    stats = lax.all_gather(stats, "chan", axis=1, tiled=True)
    gain_all, bias_all = stats[3], stats[4]
    stats = stats[:3]
    for axis in reversed(SUB):
        stats = lax.all_gather(stats, axis, axis=0, tiled=True)
    stats = stats.reshape(-1, 3, stats.shape[-1])
    sums, squares, counts = stats[:, 0], stats[:, 1], stats[:, 2]
    live_total = jnp.sum(counts[:, 0])
    average = jnp.sum(sums, axis=0) / live_total
    spread = sums / counts - average[None, :]
    variance = (jnp.sum(squares, axis=0) + jnp.sum(counts * spread * spread, axis=0)) / live_total
    factor = gain_all * lax.rsqrt(variance + 1e-05)
    halo_row = jnp.arange(border, dtype=jnp.int32)
    after_mask = (halo_row < next_live[0] - border).astype(jnp.float32)
    table_mask = jnp.concatenate([jnp.ones((border,), jnp.float32), live_mask, after_mask])
    gathered = (
        jnp.maximum((table - average[:, None]) * factor[:, None] + bias_all[:, None], 0.0)
        * table_mask[None, :]
    ).astype(jnp.bfloat16)
    anchor = region_idx * columns - border
    block_base = (column // BLOCK) * BLOCK
    rel = jnp.where(neighbors < 0, -1, neighbors - anchor - block_base[None, :])
    picked, grad_parts = gather_call(rel, gathered, grad_out, border)
    kernel_grad = lax.psum(grad_parts, SUB)
    conv_out = lax.dot_general(
        weights, picked, (((0, 2), (0, 1)), ((), ())), preferred_element_type=jnp.float32
    ).astype(jnp.bfloat16)
    return (conv_out, kernel_grad)


def sub_mesh(mesh):
    devices = np.asarray(mesh.devices)
    count = devices.shape[0]
    first = devices[:, 0]
    try:
        sizes = [len({d.coords[a] for d in first}) for a in (2, 1, 0)]
    except (AttributeError, IndexError, TypeError):
        sizes = [count, 1, 1]
    if int(np.prod(sizes)) != count:
        sizes = [count, 1, 1]
    return Mesh(devices.reshape(*sizes, devices.shape[1]), SUB + ("chan",))


def solution(mesh):
    sites = ("chan", SUB)
    return jax.shard_map(
        per_device,
        mesh=sub_mesh(mesh),
        in_specs=(
            P(*sites),
            P("chan"),
            P("chan"),
            P(SUB),
            P(None, SUB),
            P(None, "chan", None),
            P(*sites),
        ),
        out_specs=(P(*sites), P(None, "chan", None)),
        check_vma=False,
    )
```

```python
import functools

import jax
import jax.numpy as jnp
import numpy as np
from jax import lax
from jax.experimental import pallas as pl
from jax.experimental.pallas import tpu as pltpu
from jax.sharding import Mesh
from jax.sharding import PartitionSpec as P

SUB = ("z", "y", "x")
BLOCK = 256


def region_sum(x):
    for axis in reversed(SUB):
        x = lax.psum(x, axis)
    return x


def ring_gather(x, axis):
    count = lax.axis_size(axis)
    parts = [x]
    for shift in range(1, count):
        parts.append(lax.ppermute(x, axis, [(i, (i + shift) % count) for i in range(count)]))
    return jnp.concatenate(parts, axis=0)


def halo_pad(x, width, live):
    count = lax.axis_size(SUB)
    length = x.shape[1]
    up = [(i, (i + 1) % count) for i in range(count - 1)]
    down = [(j, i) for i, j in up]
    before = lax.ppermute(x[:, length - width:], SUB, up)
    after = lax.ppermute(x[:, :width], SUB, down)
    next_live = lax.ppermute(live, SUB, down)
    return jnp.concatenate([before, x, after], axis=1), next_live


def offset_kernel(rel_ref, act_ref, g_ref, picked_ref, kg_ref, *, halo, blocks):
    k = pl.program_id(0)
    window = BLOCK + 2 * halo
    rows = lax.broadcasted_iota(jnp.int32, (window, BLOCK), 0)
    for b in range(blocks):
        idx = rel_ref[pl.ds(k, 1), pl.ds(b * BLOCK, BLOCK)]
        onehot = jnp.where(rows == idx, 1.0, 0.0).astype(jnp.bfloat16)
        win = act_ref[:, pl.ds(b * BLOCK, window)]
        picked_ref[0, :, pl.ds(b * BLOCK, BLOCK)] = jnp.dot(
            win, onehot, preferred_element_type=jnp.float32
        ).astype(jnp.bfloat16)
    kg_ref[0] = lax.dot_general(
        g_ref[...], picked_ref[0], (((1,), (1,)), ((), ())), preferred_element_type=jnp.float32
    )


def gather_call(rel, act, grad_out, halo):
    offsets, columns = rel.shape
    c_all, extent = act.shape
    o_ch = grad_out.shape[0]
    kern = functools.partial(offset_kernel, halo=halo, blocks=columns // BLOCK)
    return pl.pallas_call(
        kern,
        grid=(offsets,),
        in_specs=[
            pl.BlockSpec((offsets, columns), lambda k: (0, 0)),
            pl.BlockSpec((c_all, extent), lambda k: (0, 0)),
            pl.BlockSpec((o_ch, columns), lambda k: (0, 0)),
        ],
        out_specs=[
            pl.BlockSpec((1, c_all, columns), lambda k: (k, 0, 0)),
            pl.BlockSpec((1, o_ch, c_all), lambda k: (k, 0, 0)),
        ],
        out_shape=[
            jax.ShapeDtypeStruct((offsets, c_all, columns), jnp.bfloat16),
            jax.ShapeDtypeStruct((offsets, o_ch, c_all), jnp.float32),
        ],
        compiler_params=pltpu.CompilerParams(
            dimension_semantics=("arbitrary",), vmem_limit_bytes=56 * 1024 * 1024
        ),
    )(rel, act, grad_out)


def per_device(features, gain, bias, live, neighbors, weights, grad_out):
    channels, columns = features.shape
    border = columns // 12
    region_idx = lax.axis_index(SUB)
    column = jnp.arange(columns, dtype=jnp.int32)
    raw_pad, next_live = halo_pad(features, border, live)
    table = lax.all_gather(raw_pad, "chan", axis=0, tiled=True).astype(jnp.float32)
    live_limit = live[0] - border
    live_mask = ((column < live_limit) | (column >= columns - border)).astype(jnp.float32)
    values = features.astype(jnp.float32)
    live_rows = jnp.sum(live_mask)
    local_sum = jnp.sum(values * live_mask[None, :], axis=1)
    local_mean = local_sum / live_rows
    local_dev = (values - local_mean[:, None]) * live_mask[None, :]
    local_sq = jnp.sum(local_dev * local_dev, axis=1)
    stats = jnp.stack(
        [local_sum, local_sq, jnp.broadcast_to(live_rows, local_sum.shape), gain, bias]
    )
    stats = lax.all_gather(stats, "chan", axis=1, tiled=True)
    gain_all, bias_all = stats[3], stats[4]
    stats = stats[:3]
    for axis in reversed(SUB):
        stats = ring_gather(stats, axis)
    stats = stats.reshape(-1, 3, stats.shape[-1])
    sums, squares, counts = stats[:, 0], stats[:, 1], stats[:, 2]
    live_total = jnp.sum(counts[:, 0])
    average = jnp.sum(sums, axis=0) / live_total
    spread = sums / counts - average[None, :]
    variance = (jnp.sum(squares, axis=0) + jnp.sum(counts * spread * spread, axis=0)) / live_total
    factor = gain_all * lax.rsqrt(variance + 1e-05)
    halo_row = jnp.arange(border, dtype=jnp.int32)
    after_mask = (halo_row < next_live[0] - border).astype(jnp.float32)
    table_mask = jnp.concatenate([jnp.ones((border,), jnp.float32), live_mask, after_mask])
    gathered = (
        jnp.maximum((table - average[:, None]) * factor[:, None] + bias_all[:, None], 0.0)
        * table_mask[None, :]
    ).astype(jnp.bfloat16)
    anchor = region_idx * columns - border
    block_base = (column // BLOCK) * BLOCK
    rel = jnp.where(neighbors < 0, -1, neighbors - anchor - block_base[None, :])
    picked, grad_parts = gather_call(rel, gathered, grad_out, border)
    kernel_grad = lax.psum(grad_parts, SUB)
    conv_out = lax.dot_general(
        weights, picked, (((0, 2), (0, 1)), ((), ())), preferred_element_type=jnp.float32
    ).astype(jnp.bfloat16)
    return (conv_out, kernel_grad)


def sub_mesh(mesh):
    devices = np.asarray(mesh.devices)
    count = devices.shape[0]
    first = devices[:, 0]
    try:
        sizes = [len({d.coords[a] for d in first}) for a in (2, 1, 0)]
    except (AttributeError, IndexError, TypeError):
        sizes = [count, 1, 1]
    if int(np.prod(sizes)) != count:
        sizes = [count, 1, 1]
    return Mesh(devices.reshape(*sizes, devices.shape[1]), SUB + ("chan",))


def solution(mesh):
    sites = ("chan", SUB)
    return jax.shard_map(
        per_device,
        mesh=sub_mesh(mesh),
        in_specs=(
            P(*sites),
            P("chan"),
            P("chan"),
            P(SUB),
            P(None, SUB),
            P(None, "chan", None),
            P(*sites),
        ),
        out_specs=(P(*sites), P(None, "chan", None)),
        check_vma=False,
    )
```

```python
import functools

import jax
import jax.numpy as jnp
import numpy as np
from jax import lax
from jax.experimental import pallas as pl
from jax.experimental.pallas import tpu as pltpu
from jax.sharding import Mesh
from jax.sharding import PartitionSpec as P

SUB = ("z", "y", "x")
BLOCK = 256


def region_sum(x):
    for axis in reversed(SUB):
        x = lax.psum(x, axis)
    return x


def ring_gather(x, axis):
    count = lax.axis_size(axis)
    parts = [x]
    for shift in range(1, count):
        parts.append(lax.ppermute(x, axis, [(i, (i + shift) % count) for i in range(count)]))
    return jnp.concatenate(parts, axis=0)


def halo_pad(x, width, live):
    count = lax.axis_size(SUB)
    length = x.shape[1]
    up = [(i, (i + 1) % count) for i in range(count - 1)]
    down = [(j, i) for i, j in up]
    before = lax.ppermute(x[:, length - width:], SUB, up)
    after = lax.ppermute(x[:, :width], SUB, down)
    next_live = lax.ppermute(live, SUB, down)
    return jnp.concatenate([before, x, after], axis=1), next_live


def offset_kernel(rel_ref, act_ref, g_ref, picked_ref, kg_ref, *, halo, blocks):
    k = pl.program_id(0)
    window = BLOCK + 2 * halo
    rows = lax.broadcasted_iota(jnp.int32, (window, BLOCK), 0)
    for b in range(blocks):
        idx = rel_ref[pl.ds(k, 1), pl.ds(b * BLOCK, BLOCK)]
        onehot = jnp.where(rows == idx, 1.0, 0.0).astype(jnp.bfloat16)
        win = act_ref[:, pl.ds(b * BLOCK, window)]
        picked_ref[0, :, pl.ds(b * BLOCK, BLOCK)] = jnp.dot(
            win, onehot, preferred_element_type=jnp.float32
        ).astype(jnp.bfloat16)
    kg_ref[0] = lax.dot_general(
        g_ref[...], picked_ref[0], (((1,), (1,)), ((), ())), preferred_element_type=jnp.float32
    )


def gather_call(rel, act, grad_out, halo):
    offsets, columns = rel.shape
    c_all, extent = act.shape
    o_ch = grad_out.shape[0]
    kern = functools.partial(offset_kernel, halo=halo, blocks=columns // BLOCK)
    return pl.pallas_call(
        kern,
        grid=(offsets,),
        in_specs=[
            pl.BlockSpec((offsets, columns), lambda k: (0, 0)),
            pl.BlockSpec((c_all, extent), lambda k: (0, 0)),
            pl.BlockSpec((o_ch, columns), lambda k: (0, 0)),
        ],
        out_specs=[
            pl.BlockSpec((1, c_all, columns), lambda k: (k, 0, 0)),
            pl.BlockSpec((1, o_ch, c_all), lambda k: (k, 0, 0)),
        ],
        out_shape=[
            jax.ShapeDtypeStruct((offsets, c_all, columns), jnp.bfloat16),
            jax.ShapeDtypeStruct((offsets, o_ch, c_all), jnp.float32),
        ],
        compiler_params=pltpu.CompilerParams(
            dimension_semantics=("arbitrary",), vmem_limit_bytes=56 * 1024 * 1024
        ),
    )(rel, act, grad_out)


def per_device(features, gain, bias, live, neighbors, weights, grad_out):
    channels, columns = features.shape
    border = columns // 12
    region_idx = lax.axis_index(SUB)
    column = jnp.arange(columns, dtype=jnp.int32)
    own_table = lax.all_gather(features, "chan", axis=0, tiled=True)
    raw_pad, next_live = halo_pad(own_table, border, live)
    table = raw_pad.astype(jnp.float32)
    live_limit = live[0] - border
    live_mask = ((column < live_limit) | (column >= columns - border)).astype(jnp.float32)
    values = features.astype(jnp.float32)
    live_rows = jnp.sum(live_mask)
    local_sum = jnp.sum(values * live_mask[None, :], axis=1)
    local_mean = local_sum / live_rows
    local_dev = (values - local_mean[:, None]) * live_mask[None, :]
    local_sq = jnp.sum(local_dev * local_dev, axis=1)
    stats = jnp.stack(
        [local_sum, local_sq, jnp.broadcast_to(live_rows, local_sum.shape), gain, bias]
    )
    stats = lax.all_gather(stats, "chan", axis=1, tiled=True)
    gain_all, bias_all = stats[3], stats[4]
    stats = stats[:3]
    for axis in reversed(SUB):
        stats = ring_gather(stats, axis)
    stats = stats.reshape(-1, 3, stats.shape[-1])
    sums, squares, counts = stats[:, 0], stats[:, 1], stats[:, 2]
    live_total = jnp.sum(counts[:, 0])
    average = jnp.sum(sums, axis=0) / live_total
    spread = sums / counts - average[None, :]
    variance = (jnp.sum(squares, axis=0) + jnp.sum(counts * spread * spread, axis=0)) / live_total
    factor = gain_all * lax.rsqrt(variance + 1e-05)
    halo_row = jnp.arange(border, dtype=jnp.int32)
    after_mask = (halo_row < next_live[0] - border).astype(jnp.float32)
    table_mask = jnp.concatenate([jnp.ones((border,), jnp.float32), live_mask, after_mask])
    gathered = (
        jnp.maximum((table - average[:, None]) * factor[:, None] + bias_all[:, None], 0.0)
        * table_mask[None, :]
    ).astype(jnp.bfloat16)
    anchor = region_idx * columns - border
    block_base = (column // BLOCK) * BLOCK
    rel = jnp.where(neighbors < 0, -1, neighbors - anchor - block_base[None, :])
    picked, grad_parts = gather_call(rel, gathered, grad_out, border)
    kernel_grad = lax.psum(grad_parts, SUB)
    conv_out = lax.dot_general(
        weights, picked, (((0, 2), (0, 1)), ((), ())), preferred_element_type=jnp.float32
    ).astype(jnp.bfloat16)
    return (conv_out, kernel_grad)


def sub_mesh(mesh):
    devices = np.asarray(mesh.devices)
    count = devices.shape[0]
    first = devices[:, 0]
    try:
        sizes = [len({d.coords[a] for d in first}) for a in (2, 1, 0)]
    except (AttributeError, IndexError, TypeError):
        sizes = [count, 1, 1]
    if int(np.prod(sizes)) != count:
        sizes = [count, 1, 1]
    return Mesh(devices.reshape(*sizes, devices.shape[1]), SUB + ("chan",))


def solution(mesh):
    sites = ("chan", SUB)
    return jax.shard_map(
        per_device,
        mesh=sub_mesh(mesh),
        in_specs=(
            P(*sites),
            P("chan"),
            P("chan"),
            P(SUB),
            P(None, SUB),
            P(None, "chan", None),
            P(*sites),
        ),
        out_specs=(P(*sites), P(None, "chan", None)),
        check_vma=False,
    )
```

```python
import functools

import jax
import jax.numpy as jnp
import numpy as np
from jax import lax
from jax.experimental import pallas as pl
from jax.experimental.pallas import tpu as pltpu
from jax.sharding import Mesh
from jax.sharding import PartitionSpec as P

SUB = ("z", "y", "x")
BLOCK = 256


def region_sum(x):
    for axis in reversed(SUB):
        x = lax.psum(x, axis)
    return x


def ring_gather(x, axis):
    count = lax.axis_size(axis)
    parts = [x]
    for shift in range(1, count):
        parts.append(lax.ppermute(x, axis, [(i, (i + shift) % count) for i in range(count)]))
    return jnp.concatenate(parts, axis=0)


def halo_pad(x, width, live):
    count = lax.axis_size(SUB)
    length = x.shape[1]
    up = [(i, (i + 1) % count) for i in range(count - 1)]
    down = [(j, i) for i, j in up]
    before = lax.ppermute(x[:, length - width:], SUB, up)
    after = lax.ppermute(x[:, :width], SUB, down)
    next_live = lax.ppermute(live, SUB, down)
    return jnp.concatenate([before, x, after], axis=1), next_live


def offset_kernel(rel_ref, act_ref, g_ref, picked_ref, kg_ref, *, halo, blocks, group):
    step = pl.program_id(0)
    window = BLOCK + 2 * halo
    rows = lax.broadcasted_iota(jnp.int32, (window, BLOCK), 0)
    for j in range(group):
        k = step * group + j
        for b in range(blocks):
            idx = rel_ref[pl.ds(k, 1), pl.ds(b * BLOCK, BLOCK)]
            onehot = jnp.where(rows == idx, 1.0, 0.0).astype(jnp.bfloat16)
            win = act_ref[:, pl.ds(b * BLOCK, window)]
            picked_ref[j, :, pl.ds(b * BLOCK, BLOCK)] = jnp.dot(
                win, onehot, preferred_element_type=jnp.float32
            ).astype(jnp.bfloat16)
        kg_ref[j] = lax.dot_general(
            g_ref[...], picked_ref[j], (((1,), (1,)), ((), ())), preferred_element_type=jnp.float32
        )


def gather_call(rel, act, grad_out, halo):
    offsets, columns = rel.shape
    c_all, extent = act.shape
    o_ch = grad_out.shape[0]
    group = 3 if offsets % 3 == 0 else 1
    kern = functools.partial(offset_kernel, halo=halo, blocks=columns // BLOCK, group=group)
    return pl.pallas_call(
        kern,
        grid=(offsets // group,),
        in_specs=[
            pl.BlockSpec((offsets, columns), lambda k: (0, 0)),
            pl.BlockSpec((c_all, extent), lambda k: (0, 0)),
            pl.BlockSpec((o_ch, columns), lambda k: (0, 0)),
        ],
        out_specs=[
            pl.BlockSpec((group, c_all, columns), lambda k: (k, 0, 0)),
            pl.BlockSpec((group, o_ch, c_all), lambda k: (k, 0, 0)),
        ],
        out_shape=[
            jax.ShapeDtypeStruct((offsets, c_all, columns), jnp.bfloat16),
            jax.ShapeDtypeStruct((offsets, o_ch, c_all), jnp.float32),
        ],
        compiler_params=pltpu.CompilerParams(
            dimension_semantics=("arbitrary",), vmem_limit_bytes=56 * 1024 * 1024
        ),
    )(rel, act, grad_out)


def per_device(features, gain, bias, live, neighbors, weights, grad_out):
    channels, columns = features.shape
    border = columns // 12
    region_idx = lax.axis_index(SUB)
    column = jnp.arange(columns, dtype=jnp.int32)
    own_table = lax.all_gather(features, "chan", axis=0, tiled=True)
    raw_pad, next_live = halo_pad(own_table, border, live)
    table = raw_pad.astype(jnp.float32)
    live_limit = live[0] - border
    live_mask = ((column < live_limit) | (column >= columns - border)).astype(jnp.float32)
    values = features.astype(jnp.float32)
    live_rows = jnp.sum(live_mask)
    local_sum = jnp.sum(values * live_mask[None, :], axis=1)
    local_mean = local_sum / live_rows
    local_dev = (values - local_mean[:, None]) * live_mask[None, :]
    local_sq = jnp.sum(local_dev * local_dev, axis=1)
    stats = jnp.stack(
        [local_sum, local_sq, jnp.broadcast_to(live_rows, local_sum.shape), gain, bias]
    )
    stats = lax.all_gather(stats, "chan", axis=1, tiled=True)
    gain_all, bias_all = stats[3], stats[4]
    stats = stats[:3]
    for axis in reversed(SUB):
        stats = ring_gather(stats, axis)
    stats = stats.reshape(-1, 3, stats.shape[-1])
    sums, squares, counts = stats[:, 0], stats[:, 1], stats[:, 2]
    live_total = jnp.sum(counts[:, 0])
    average = jnp.sum(sums, axis=0) / live_total
    spread = sums / counts - average[None, :]
    variance = (jnp.sum(squares, axis=0) + jnp.sum(counts * spread * spread, axis=0)) / live_total
    factor = gain_all * lax.rsqrt(variance + 1e-05)
    halo_row = jnp.arange(border, dtype=jnp.int32)
    after_mask = (halo_row < next_live[0] - border).astype(jnp.float32)
    table_mask = jnp.concatenate([jnp.ones((border,), jnp.float32), live_mask, after_mask])
    gathered = (
        jnp.maximum((table - average[:, None]) * factor[:, None] + bias_all[:, None], 0.0)
        * table_mask[None, :]
    ).astype(jnp.bfloat16)
    anchor = region_idx * columns - border
    block_base = (column // BLOCK) * BLOCK
    rel = jnp.where(neighbors < 0, -1, neighbors - anchor - block_base[None, :])
    picked, grad_parts = gather_call(rel, gathered, grad_out, border)
    kernel_grad = lax.psum(grad_parts, SUB)
    conv_out = lax.dot_general(
        weights, picked, (((0, 2), (0, 1)), ((), ())), preferred_element_type=jnp.float32
    ).astype(jnp.bfloat16)
    return (conv_out, kernel_grad)


def sub_mesh(mesh):
    devices = np.asarray(mesh.devices)
    count = devices.shape[0]
    first = devices[:, 0]
    try:
        sizes = [len({d.coords[a] for d in first}) for a in (2, 1, 0)]
    except (AttributeError, IndexError, TypeError):
        sizes = [count, 1, 1]
    if int(np.prod(sizes)) != count:
        sizes = [count, 1, 1]
    return Mesh(devices.reshape(*sizes, devices.shape[1]), SUB + ("chan",))


def solution(mesh):
    sites = ("chan", SUB)
    return jax.shard_map(
        per_device,
        mesh=sub_mesh(mesh),
        in_specs=(
            P(*sites),
            P("chan"),
            P("chan"),
            P(SUB),
            P(None, SUB),
            P(None, "chan", None),
            P(*sites),
        ),
        out_specs=(P(*sites), P(None, "chan", None)),
        check_vma=False,
    )
```

```python
import functools

import jax
import jax.numpy as jnp
import numpy as np
from jax import lax
from jax.experimental import pallas as pl
from jax.experimental.pallas import tpu as pltpu
from jax.sharding import Mesh
from jax.sharding import PartitionSpec as P

SUB = ("z", "y", "x")
BLOCK = 256


def region_sum(x):
    for axis in reversed(SUB):
        x = lax.psum(x, axis)
    return x


def ring_gather(x, axis):
    count = lax.axis_size(axis)
    parts = [x]
    for shift in range(1, count):
        parts.append(lax.ppermute(x, axis, [(i, (i + shift) % count) for i in range(count)]))
    return jnp.concatenate(parts, axis=0)


def halo_pad(x, width, live):
    count = lax.axis_size(SUB)
    length = x.shape[1]
    up = [(i, (i + 1) % count) for i in range(count - 1)]
    down = [(j, i) for i, j in up]
    before = lax.ppermute(x[:, length - width:], SUB, up)
    after = lax.ppermute(x[:, :width], SUB, down)
    next_live = lax.ppermute(live, SUB, down)
    return jnp.concatenate([before, x, after], axis=1), next_live


def offset_kernel(rel_ref, act_ref, g_ref, picked_ref, kg_ref, *, halo, blocks, group):
    step = pl.program_id(0)
    window = BLOCK + 2 * halo
    rows = lax.broadcasted_iota(jnp.int32, (window, BLOCK), 0)
    for j in range(group):
        k = step * group + j
        for b in range(blocks):
            idx = rel_ref[pl.ds(k, 1), pl.ds(b * BLOCK, BLOCK)]
            onehot = jnp.where(rows == idx, 1.0, 0.0).astype(jnp.bfloat16)
            win = act_ref[:, pl.ds(b * BLOCK, window)]
            picked_ref[j, :, pl.ds(b * BLOCK, BLOCK)] = jnp.dot(
                win, onehot, preferred_element_type=jnp.float32
            ).astype(jnp.bfloat16)
        kg_ref[j] = lax.dot_general(
            g_ref[...], picked_ref[j], (((1,), (1,)), ((), ())), preferred_element_type=jnp.float32
        )


def gather_call(rel, act, grad_out, halo):
    offsets, columns = rel.shape
    c_all, extent = act.shape
    o_ch = grad_out.shape[0]
    group = 9 if offsets % 9 == 0 else 1
    kern = functools.partial(offset_kernel, halo=halo, blocks=columns // BLOCK, group=group)
    return pl.pallas_call(
        kern,
        grid=(offsets // group,),
        in_specs=[
            pl.BlockSpec((offsets, columns), lambda k: (0, 0)),
            pl.BlockSpec((c_all, extent), lambda k: (0, 0)),
            pl.BlockSpec((o_ch, columns), lambda k: (0, 0)),
        ],
        out_specs=[
            pl.BlockSpec((group, c_all, columns), lambda k: (k, 0, 0)),
            pl.BlockSpec((group, o_ch, c_all), lambda k: (k, 0, 0)),
        ],
        out_shape=[
            jax.ShapeDtypeStruct((offsets, c_all, columns), jnp.bfloat16),
            jax.ShapeDtypeStruct((offsets, o_ch, c_all), jnp.float32),
        ],
        compiler_params=pltpu.CompilerParams(
            dimension_semantics=("arbitrary",), vmem_limit_bytes=56 * 1024 * 1024
        ),
    )(rel, act, grad_out)


def per_device(features, gain, bias, live, neighbors, weights, grad_out):
    channels, columns = features.shape
    border = columns // 12
    region_idx = lax.axis_index(SUB)
    column = jnp.arange(columns, dtype=jnp.int32)
    own_table = lax.all_gather(features, "chan", axis=0, tiled=True)
    raw_pad, next_live = halo_pad(own_table, border, live)
    table = raw_pad.astype(jnp.float32)
    live_limit = live[0] - border
    live_mask = ((column < live_limit) | (column >= columns - border)).astype(jnp.float32)
    values = features.astype(jnp.float32)
    live_rows = jnp.sum(live_mask)
    local_sum = jnp.sum(values * live_mask[None, :], axis=1)
    local_mean = local_sum / live_rows
    local_dev = (values - local_mean[:, None]) * live_mask[None, :]
    local_sq = jnp.sum(local_dev * local_dev, axis=1)
    stats = jnp.stack(
        [local_sum, local_sq, jnp.broadcast_to(live_rows, local_sum.shape), gain, bias]
    )
    stats = lax.all_gather(stats, "chan", axis=1, tiled=True)
    gain_all, bias_all = stats[3], stats[4]
    stats = stats[:3]
    for axis in reversed(SUB):
        stats = ring_gather(stats, axis)
    stats = stats.reshape(-1, 3, stats.shape[-1])
    sums, squares, counts = stats[:, 0], stats[:, 1], stats[:, 2]
    live_total = jnp.sum(counts[:, 0])
    average = jnp.sum(sums, axis=0) / live_total
    spread = sums / counts - average[None, :]
    variance = (jnp.sum(squares, axis=0) + jnp.sum(counts * spread * spread, axis=0)) / live_total
    factor = gain_all * lax.rsqrt(variance + 1e-05)
    halo_row = jnp.arange(border, dtype=jnp.int32)
    after_mask = (halo_row < next_live[0] - border).astype(jnp.float32)
    table_mask = jnp.concatenate([jnp.ones((border,), jnp.float32), live_mask, after_mask])
    gathered = (
        jnp.maximum((table - average[:, None]) * factor[:, None] + bias_all[:, None], 0.0)
        * table_mask[None, :]
    ).astype(jnp.bfloat16)
    anchor = region_idx * columns - border
    block_base = (column // BLOCK) * BLOCK
    rel = jnp.where(neighbors < 0, -1, neighbors - anchor - block_base[None, :])
    picked, grad_parts = gather_call(rel, gathered, grad_out, border)
    kernel_grad = lax.psum(grad_parts, SUB)
    conv_out = lax.dot_general(
        weights, picked, (((0, 2), (0, 1)), ((), ())), preferred_element_type=jnp.float32
    ).astype(jnp.bfloat16)
    return (conv_out, kernel_grad)


def sub_mesh(mesh):
    devices = np.asarray(mesh.devices)
    count = devices.shape[0]
    first = devices[:, 0]
    try:
        sizes = [len({d.coords[a] for d in first}) for a in (2, 1, 0)]
    except (AttributeError, IndexError, TypeError):
        sizes = [count, 1, 1]
    if int(np.prod(sizes)) != count:
        sizes = [count, 1, 1]
    return Mesh(devices.reshape(*sizes, devices.shape[1]), SUB + ("chan",))


def solution(mesh):
    sites = ("chan", SUB)
    return jax.shard_map(
        per_device,
        mesh=sub_mesh(mesh),
        in_specs=(
            P(*sites),
            P("chan"),
            P("chan"),
            P(SUB),
            P(None, SUB),
            P(None, "chan", None),
            P(*sites),
        ),
        out_specs=(P(*sites), P(None, "chan", None)),
        check_vma=False,
    )
```
